32 devices in a mesh: shots: 2 (over x), src: 16 (over z, y, core).
Axes of the slice: x: 2, y: 2, z: 4, core: 2. Of those that a mesh axis runs over, the one named last changes fastest.
Arguments:
- weights_in: float32 [1024, 128, 256], P(('shots', 'src')), parts along dimension 0, may hold values from -6 to 6
- translations: float32 [8, 8, 2, 2, 64, 64], replicated, may hold values from -0.375 to 0.375
- pattern_index: int32 [8, 512], replicated, may hold values from 0 to 7
Outputs:
- weights_out: float32 [1024, 128, 256], P(('shots', 'src')), parts along dimension 0
The draws below stay inside these ranges and needn't reach their ends.
There are 2 independent parts, one for each index of `shots`. The reference program is written for one: setup_inputs(seed, part) draws one part's arguments, and reference() takes and returns one part's arrays. A program takes and returns all parts, laid end to end along the dimension named above; an argument that names none is the same for every part. Nothing has to cross between parts.
All inputs are finite; a program needn't handle non-finite values.
Results may differ from the reference program's by a relative error of at most 0.0001.
Values sent between devices are 32-bit elements; how exact they have to be, the bound alone decides.
No kernel may reach another device: no remote copies, remote signals or barrier semaphores. Data moves between devices by JAX's collectives and lax.ppermute only.
A program may use at most 128 MiB of HBM per device.

```python
import jax
import jax.numpy as jnp
from jax import lax

RANK = 64
K = 256
LEVELS = 8
PATTERNS = 8
BOXES = 512


def place_ends(array, own_key, least, top_value):
    index_at = [jax.random.randint(jax.random.fold_in(own_key, axis), (), 0, length) for axis, length in enumerate(array.shape)]
    longest = array.shape.index(max(array.shape))
    neighbour = index_at[:longest] + [(index_at[longest] + 1) % array.shape[longest]] + index_at[longest + 1:]
    return array.at[tuple(index_at)].set(least).at[tuple(neighbour)].set(top_value)


def level_of(key, shape, cuts, least, top_value):
    loudness, own = 1.0, jax.random.fold_in(key, 6)
    for dim, blocks in cuts:
        steps = jnp.exp(jax.random.uniform(jax.random.fold_in(own, dim), (blocks,), jnp.float32, least / len(cuts), top_value / len(cuts)))
        loudness = loudness * jnp.repeat(steps, shape[dim] // blocks).reshape([-1 if axis == dim else 1 for axis in range(len(shape))])
    return loudness


def gaussian(stream_key, dims, scale, bound, shards=(), held_as=jnp.bfloat16):
    values = scale * jax.random.normal(stream_key, dims, jnp.float32)
    if shards:
        values = values * level_of(stream_key, dims, shards, -0.22, 0.18)
    return jnp.clip(values, -bound, bound).astype(held_as)


def setup_inputs(seed: int = 0, part: int = 0) -> dict:
    keys = jax.random.split(jax.random.key(seed), 4)
    part_splits = jax.random.split(jax.random.fold_in(keys[3], part), 4)
    weights_in = gaussian(part_splits[0], (BOXES, 2 * RANK, K), 1.0, 6.0, ((0, 16),), jnp.float32)
    translations = gaussian(keys[1], (LEVELS, PATTERNS, 2, 2, RANK, RANK), (4 * RANK) ** -0.5, 0.375, (), jnp.float32)
    pattern_index = place_ends(jax.random.randint(keys[2], (LEVELS, BOXES), 0, PATTERNS), jax.random.fold_in(keys[2], 1), 0, PATTERNS - 1).astype(jnp.int32)
    return dict(weights_in=weights_in, translations=translations, pattern_index=pattern_index)


def pair_flip(field, bit):
    count = field.shape[0]
    shaped = field.reshape((count // (2 << bit), 2, 1 << bit) + field.shape[1:])
    return jnp.flip(shaped, 1).reshape(field.shape)


def block_real(chosen):
    real_part = chosen[:, :, 0]
    imag_part = chosen[:, :, 1]
    upper = jnp.concatenate([real_part, -imag_part], axis=-1)
    lower = jnp.concatenate([imag_part, real_part], axis=-1)
    return jnp.concatenate([upper, lower], axis=-2)


def reference(weights_in, translations, pattern_index):
    top_bits = BOXES.bit_length() - 1
    state = weights_in.astype(jnp.float32)
    for level in range(LEVELS):
        bit = top_bits - LEVELS + level
        other = pair_flip(state, bit)
        chosen = jnp.take(translations[level], pattern_index[level], axis=0)
        mats = block_real(chosen)
        state = jnp.einsum("bij,bjk->bik", mats[:, 0], state, precision=lax.Precision.HIGHEST) + jnp.einsum("bij,bjk->bik", mats[:, 1], other, precision=lax.Precision.HIGHEST)
    return state
```

```python
import functools

import jax
import jax.numpy as jnp
from jax import lax
from jax.experimental import pallas as pl
from jax.experimental.pallas import tpu as pltpu
from jax.sharding import PartitionSpec as P

LEVELS = 8
K_CHUNKS = 2


def block_real_table(translations):
    real_part = translations[:, :, :, 0]
    imag_part = translations[:, :, :, 1]
    upper = jnp.concatenate([real_part, -imag_part], axis=-1)
    lower = jnp.concatenate([imag_part, real_part], axis=-1)
    return jnp.concatenate([upper, lower], axis=-2)


def levels_kernel(masks, pidx_ref, m_ref, x_ref, o_ref, buf):
    count = x_ref.shape[0]
    src = x_ref
    for li, mask in enumerate(masks):
        dst = o_ref if li == len(masks) - 1 else buf.at[li % 2]

        def pair(i, carry, src=src, dst=dst, li=li, mask=mask):
            lo = (i // mask) * (2 * mask) + i % mask
            hi = lo + mask
            p_lo = pidx_ref[li, lo]
            p_hi = pidx_ref[li, hi]
            lhs = jnp.concatenate(
                [
                    jnp.concatenate([m_ref[li, p_lo, 0], m_ref[li, p_lo, 1]], axis=1),
                    jnp.concatenate([m_ref[li, p_hi, 1], m_ref[li, p_hi, 0]], axis=1),
                ],
                axis=0,
            )
            rhs = jnp.concatenate([src[lo], src[hi]], axis=0)
            out = jnp.dot(lhs, rhs, precision=lax.Precision.HIGHEST, preferred_element_type=jnp.float32)
            half = out.shape[0] // 2
            dst[lo] = out[:half]
            dst[hi] = out[half:]
            return carry

        lax.fori_loop(0, count // 2, pair, 0)
        src = dst


def apply_levels(state, mats, pidx, masks, chunk, width):
    count, rows, _ = state.shape
    n_levels = mats.shape[0]
    kernel = functools.partial(levels_kernel, tuple(masks))
    flops = 2 * count * rows * 2 * rows * width * n_levels
    return pl.pallas_call(
        kernel,
        out_shape=jax.ShapeDtypeStruct((count, rows, width), state.dtype),
        grid_spec=pltpu.PrefetchScalarGridSpec(
            num_scalar_prefetch=1,
            grid=(1,),
            in_specs=[
                pl.BlockSpec(mats.shape, lambda i, p: (0,) * mats.ndim),
                pl.BlockSpec((count, rows, width), lambda i, p: (0, 0, chunk)),
            ],
            out_specs=pl.BlockSpec((count, rows, width), lambda i, p: (0, 0, 0)),
            scratch_shapes=[pltpu.VMEM((2, count, rows, width), jnp.float32)],
        ),
        compiler_params=pltpu.CompilerParams(vmem_limit_bytes=60 * 1024 * 1024),
        cost_estimate=pl.CostEstimate(
            flops=flops, transcendentals=0, bytes_accessed=2 * count * rows * width * 4 + mats.size * 4
        ),
    )(pidx, mats, state)


def body(weights_in, translations, pattern_index):
    box_count, rows, k_len = weights_in.shape
    groups = lax.axis_size("src")
    local_bits = box_count.bit_length() - 1
    top_bits = (box_count * groups).bit_length() - 1
    device = lax.axis_index("src")
    mats = block_real_table(translations)
    bits = [top_bits - LEVELS + level for level in range(LEVELS)]
    first_cross = next((lv for lv, b in enumerate(bits) if b >= local_bits), LEVELS)

    own_boxes = device * box_count + jnp.arange(box_count, dtype=jnp.int32)
    repeat = box_count // groups
    repeat_bits = repeat.bit_length() - 1
    slot = jnp.arange(box_count, dtype=jnp.int32)
    held_boxes = slot // repeat * box_count + device * repeat + slot % repeat

    width = k_len // K_CHUNKS
    local_masks = [1 << bits[lv] for lv in range(first_cross)]
    cross_masks = [1 << (bits[lv] - local_bits + repeat_bits) for lv in range(first_cross, LEVELS)]
    local_pidx = jnp.take(pattern_index[:first_cross], own_boxes, axis=1)
    cross_pidx = jnp.take(pattern_index[first_cross:], held_boxes, axis=1)

    pieces = []
    for chunk in range(K_CHUNKS):
        if first_cross > 0:
            state = apply_levels(weights_in, mats[:first_cross], local_pidx, local_masks, chunk, width)
            src_chunk = 0
        else:
            state = weights_in
            src_chunk = chunk
        current = lax.all_to_all(state, "src", split_axis=0, concat_axis=0, tiled=True)
        current = apply_levels(current, mats[first_cross:], cross_pidx, cross_masks, src_chunk, width)
        pieces.append(lax.all_to_all(current, "src", split_axis=0, concat_axis=0, tiled=True))
    return jnp.concatenate(pieces, axis=-1)


def solution(mesh):
    placed = (P(("shots", "src"), None, None), P(), P())
    return jax.shard_map(
        body, mesh=mesh, in_specs=placed, out_specs=P(("shots", "src"), None, None), check_vma=False
    )
```

```python
import functools

import jax
import jax.numpy as jnp
from jax import lax
from jax.experimental import pallas as pl
from jax.experimental.pallas import tpu as pltpu
from jax.sharding import PartitionSpec as P

LEVELS = 8
K_CHUNKS = 2
PARITY_SPLIT = True


def levels_kernel(masks, pidx_ref, tr_ref, x_ref, o_ref, table, buf):
    level = pl.program_id(0)
    patterns = tr_ref.shape[1]
    rank = tr_ref.shape[4]
    for p in range(patterns):
        for j in range(2):
            re = tr_ref[0, p, j, 0]
            im = tr_ref[0, p, j, 1]
            table[p, j, 0:rank] = re - pltpu.roll(im, rank, 1)
            table[p, j, rank : 2 * rank] = im + pltpu.roll(re, rank, 1)

    count = x_ref.shape[0]
    last = len(masks) - 1
    for li, mask in enumerate(masks):
        src = x_ref if li == 0 else buf.at[(li - 1) % 2]
        dst = o_ref if li == last else buf.at[li % 2]

        @pl.when(level == li)
        def _(src=src, dst=dst, li=li, mask=mask):
            def pair(i, carry):
                lo = (i // mask) * (2 * mask) + i % mask
                hi = lo + mask
                p_lo = pidx_ref[li, lo]
                p_hi = pidx_ref[li, hi]
                lhs = jnp.concatenate(
                    [
                        jnp.concatenate([table[p_lo, 0], table[p_lo, 1]], axis=1),
                        jnp.concatenate([table[p_hi, 1], table[p_hi, 0]], axis=1),
                    ],
                    axis=0,
                )
                rhs = jnp.concatenate([src[lo], src[hi]], axis=0)
                out = jnp.dot(lhs, rhs, precision=lax.Precision.HIGHEST, preferred_element_type=jnp.float32)
                half = out.shape[0] // 2
                dst[lo] = out[:half]
                dst[hi] = out[half:]
                return carry

            lax.fori_loop(0, count // 2, pair, 0)


def apply_levels(state, trp, pidx, masks, level_offset, index_of, count, width):
    rows = state.shape[-2]
    n_levels = len(masks)
    patterns = trp.shape[1]
    rank = trp.shape[4]
    block = (count, None, rows, width) if state.ndim == 4 else (count, rows, width)
    flops = 2 * count * rows * 2 * rows * width * n_levels
    return pl.pallas_call(
        functools.partial(levels_kernel, tuple(masks)),
        out_shape=jax.ShapeDtypeStruct((count, rows, width), state.dtype),
        grid_spec=pltpu.PrefetchScalarGridSpec(
            num_scalar_prefetch=1,
            grid=(n_levels,),
            in_specs=[
                pl.BlockSpec((1,) + trp.shape[1:], lambda i, p: (level_offset + i, 0, 0, 0, 0, 0)),
                pl.BlockSpec(block, lambda i, p: index_of),
            ],
            out_specs=pl.BlockSpec((count, rows, width), lambda i, p: (0, 0, 0)),
            scratch_shapes=[
                pltpu.VMEM((patterns, 2, 2 * rank, 2 * rank), jnp.float32),
                pltpu.VMEM((2, count, rows, width), jnp.float32),
            ],
        ),
        compiler_params=pltpu.CompilerParams(vmem_limit_bytes=48 * 1024 * 1024),
        cost_estimate=pl.CostEstimate(
            flops=flops, transcendentals=0, bytes_accessed=2 * count * rows * width * 4 + n_levels * trp[0].size * 4
        ),
    )(pidx, trp, state)


def body(weights_in, translations, pattern_index):
    box_count, rows, k_len = weights_in.shape
    groups = lax.axis_size("src")
    local_bits = box_count.bit_length() - 1
    top_bits = (box_count * groups).bit_length() - 1
    device = lax.axis_index("src")
    rank = translations.shape[-1]
    trp = jnp.pad(translations, [(0, 0)] * 5 + [(0, rank)])
    bits = [top_bits - LEVELS + level for level in range(LEVELS)]
    first_cross = next((lv for lv, b in enumerate(bits) if b >= local_bits), LEVELS)

    split = 2 if (PARITY_SPLIT and bits[0] >= 1 and box_count // 2 >= groups) else 1
    split_bits = split.bit_length() - 1
    count = box_count // split
    repeat = count // groups
    repeat_bits = repeat.bit_length() - 1
    width = k_len // K_CHUNKS
    shaped = weights_in.reshape(count, split, rows, k_len) if split > 1 else weights_in

    slot = jnp.arange(count, dtype=jnp.int32)
    local_masks = [1 << (bits[lv] - split_bits) for lv in range(first_cross)]
    cross_masks = [1 << (bits[lv] - local_bits + repeat_bits) for lv in range(first_cross, LEVELS)]

    pieces = {}
    for parity in range(split):
        own_boxes = device * box_count + slot * split + parity
        held_boxes = slot // repeat * box_count + (device * repeat + slot % repeat) * split + parity
        local_pidx = jnp.take(pattern_index[:first_cross], own_boxes, axis=1)
        cross_pidx = jnp.take(pattern_index[first_cross:], held_boxes, axis=1)
        for chunk in range(K_CHUNKS):
            index_of = (0, parity, 0, chunk) if split > 1 else (0, 0, chunk)
            if first_cross > 0:
                state = apply_levels(shaped, trp, local_pidx, local_masks, 0, index_of, count, width)
            elif split > 1:
                state = shaped[:, parity, :, chunk * width : (chunk + 1) * width]
            else:
                state = shaped[:, :, chunk * width : (chunk + 1) * width]
            current = lax.all_to_all(state, "src", split_axis=0, concat_axis=0, tiled=True)
            current = apply_levels(
                current, trp, cross_pidx, cross_masks, first_cross, (0, 0, 0), count, width
            )
            pieces[parity, chunk] = lax.all_to_all(current, "src", split_axis=0, concat_axis=0, tiled=True)
    joined = [jnp.concatenate([pieces[parity, c] for c in range(K_CHUNKS)], axis=-1) for parity in range(split)]
    if split > 1:
        return jnp.stack(joined, axis=1).reshape(box_count, rows, k_len)
    return joined[0]


def solution(mesh):
    placed = (P(("shots", "src"), None, None), P(), P())
    return jax.shard_map(
        body, mesh=mesh, in_specs=placed, out_specs=P(("shots", "src"), None, None), check_vma=False
    )
```

```python
import functools

import jax
import jax.numpy as jnp
from jax import lax
from jax.experimental import pallas as pl
from jax.experimental.pallas import tpu as pltpu
from jax.sharding import PartitionSpec as P

LEVELS = 8
K_CHUNKS = 2
PARITY_SPLIT = True


def levels_kernel(masks, pidx_ref, tr_ref, x_ref, o_ref, table, buf):
    level = pl.program_id(0)
    patterns = tr_ref.shape[1]
    rank = tr_ref.shape[-1]
    for p in range(patterns):
        for j in range(2):
            re = tr_ref[0, p, j, 0]
            im = tr_ref[0, p, j, 1]
            table[p, j, 0:rank] = jnp.concatenate([re, -im], axis=1)
            table[p, j, rank : 2 * rank] = jnp.concatenate([im, re], axis=1)

    count = x_ref.shape[0]
    last = len(masks) - 1
    for li, mask in enumerate(masks):
        src = x_ref if li == 0 else buf.at[(li - 1) % 2]
        dst = o_ref if li == last else buf.at[li % 2]

        @pl.when(level == li)
        def _(src=src, dst=dst, li=li, mask=mask):
            def pair(i, carry):
                lo = (i // mask) * (2 * mask) + i % mask
                hi = lo + mask
                p_lo = pidx_ref[li, lo]
                p_hi = pidx_ref[li, hi]
                lhs = jnp.concatenate(
                    [
                        jnp.concatenate([table[p_lo, 0], table[p_lo, 1]], axis=1),
                        jnp.concatenate([table[p_hi, 1], table[p_hi, 0]], axis=1),
                    ],
                    axis=0,
                )
                rhs = jnp.concatenate([src[lo], src[hi]], axis=0)
                out = jnp.dot(lhs, rhs, precision=lax.Precision.HIGHEST, preferred_element_type=jnp.float32)
                half = out.shape[0] // 2
                dst[lo] = out[:half]
                dst[hi] = out[half:]
                return carry

            lax.fori_loop(0, count // 2, pair, 0)


def apply_levels(state, trp, pidx, masks, level_offset, index_of, count, width):
    rows = state.shape[-2]
    n_levels = len(masks)
    patterns = trp.shape[1]
    rank = trp.shape[-1]
    block = (count, None, rows, width) if state.ndim == 4 else (count, rows, width)
    flops = 2 * count * rows * 2 * rows * width * n_levels
    return pl.pallas_call(
        functools.partial(levels_kernel, tuple(masks)),
        out_shape=jax.ShapeDtypeStruct((count, rows, width), state.dtype),
        grid_spec=pltpu.PrefetchScalarGridSpec(
            num_scalar_prefetch=1,
            grid=(n_levels,),
            in_specs=[
                pl.BlockSpec((1,) + trp.shape[1:], lambda i, p: (level_offset + i, 0, 0, 0, 0, 0)),
                pl.BlockSpec(block, lambda i, p: index_of),
            ],
            out_specs=pl.BlockSpec((count, rows, width), lambda i, p: (0, 0, 0)),
            scratch_shapes=[
                pltpu.VMEM((patterns, 2, 2 * rank, 2 * rank), jnp.float32),
                pltpu.VMEM((2, count, rows, width), jnp.float32),
            ],
        ),
        compiler_params=pltpu.CompilerParams(vmem_limit_bytes=48 * 1024 * 1024),
        cost_estimate=pl.CostEstimate(
            flops=flops, transcendentals=0, bytes_accessed=2 * count * rows * width * 4 + n_levels * trp[0].size * 4
        ),
    )(pidx, trp, state)


def body(weights_in, translations, pattern_index):
    box_count, rows, k_len = weights_in.shape
    groups = lax.axis_size("src")
    local_bits = box_count.bit_length() - 1
    top_bits = (box_count * groups).bit_length() - 1
    device = lax.axis_index("src")
    bits = [top_bits - LEVELS + level for level in range(LEVELS)]
    first_cross = next((lv for lv, b in enumerate(bits) if b >= local_bits), LEVELS)

    split = 2 if (PARITY_SPLIT and bits[0] >= 1 and box_count // 2 >= groups) else 1
    split_bits = split.bit_length() - 1
    count = box_count // split
    repeat = count // groups
    repeat_bits = repeat.bit_length() - 1
    k_chunks = 1 if split > 1 else K_CHUNKS
    width = k_len // k_chunks
    shaped = weights_in.reshape(count, split, rows, k_len) if split > 1 else weights_in

    slot = jnp.arange(count, dtype=jnp.int32)
    local_masks = [1 << (bits[lv] - split_bits) for lv in range(first_cross)]
    cross_masks = [1 << (bits[lv] - local_bits + repeat_bits) for lv in range(first_cross, LEVELS)]

    pieces = {}
    for parity in range(split):
        own_boxes = device * box_count + slot * split + parity
        held_boxes = slot // repeat * box_count + (device * repeat + slot % repeat) * split + parity
        local_pidx = jnp.take(pattern_index[:first_cross], own_boxes, axis=1)
        cross_pidx = jnp.take(pattern_index[first_cross:], held_boxes, axis=1)
        for chunk in range(k_chunks):
            index_of = (0, parity, 0, chunk) if split > 1 else (0, 0, chunk)
            if first_cross > 0:
                state = apply_levels(shaped, translations, local_pidx, local_masks, 0, index_of, count, width)
            elif split > 1:
                state = shaped[:, parity, :, chunk * width : (chunk + 1) * width]
            else:
                state = shaped[:, :, chunk * width : (chunk + 1) * width]
            current = lax.all_to_all(state, "src", split_axis=0, concat_axis=0, tiled=True)
            current = apply_levels(
                current, translations, cross_pidx, cross_masks, first_cross, (0, 0, 0), count, width
            )
            pieces[parity, chunk] = lax.all_to_all(current, "src", split_axis=0, concat_axis=0, tiled=True)
    joined = [jnp.concatenate([pieces[parity, c] for c in range(k_chunks)], axis=-1) for parity in range(split)]
    if split > 1:
        return jnp.stack(joined, axis=1).reshape(box_count, rows, k_len)
    return joined[0]


def solution(mesh):
    placed = (P(("shots", "src"), None, None), P(), P())
    return jax.shard_map(
        body, mesh=mesh, in_specs=placed, out_specs=P(("shots", "src"), None, None), check_vma=False
    )
```

```python
import functools

import jax
import jax.numpy as jnp
from jax import lax
from jax.experimental import pallas as pl
from jax.experimental.pallas import tpu as pltpu
from jax.sharding import PartitionSpec as P

LEVELS = 8
K_CHUNKS = 2
PARITY_SPLIT = True


def levels_kernel(masks, pidx_ref, tr_ref, x_ref, o_ref, table, buf):
    level = pl.program_id(0)
    patterns = tr_ref.shape[1]
    rank = tr_ref.shape[-1]
    for p in range(patterns):
        for j in range(2):
            re = tr_ref[0, p, j, 0]
            im = tr_ref[0, p, j, 1]
            table[p, j, 0:rank] = jnp.concatenate([re, -im], axis=1)
            table[p, j, rank : 2 * rank] = jnp.concatenate([im, re], axis=1)

    count = x_ref.shape[0]
    last = len(masks) - 1
    for li, mask in enumerate(masks):
        src = x_ref if li == 0 else buf.at[(li - 1) % 2]
        dst = o_ref if li == last else buf.at[li % 2]

        @pl.when(level == li)
        def _(src=src, dst=dst, li=li, mask=mask):
            def pair(i, carry):
                lo = (i // mask) * (2 * mask) + i % mask
                hi = lo + mask
                p_lo = pidx_ref[li, lo]
                p_hi = pidx_ref[li, hi]
                lhs = jnp.concatenate(
                    [
                        jnp.concatenate([table[p_lo, 0], table[p_lo, 1]], axis=1),
                        jnp.concatenate([table[p_hi, 1], table[p_hi, 0]], axis=1),
                    ],
                    axis=0,
                )
                rhs = jnp.concatenate([src[lo], src[hi]], axis=0)
                out = jnp.dot(lhs, rhs, precision=lax.Precision.HIGHEST, preferred_element_type=jnp.float32)
                half = out.shape[0] // 2
                dst[lo] = out[:half]
                dst[hi] = out[half:]
                return carry

            lax.fori_loop(0, count // 2, pair, 0)


def apply_levels(state, trp, pidx, masks, level_offset, index_of, count, width):
    rows = state.shape[-2]
    n_levels = len(masks)
    patterns = trp.shape[1]
    rank = trp.shape[-1]
    block = (count, None, rows, width) if state.ndim == 4 else (count, rows, width)
    flops = 2 * count * rows * 2 * rows * width * n_levels
    return pl.pallas_call(
        functools.partial(levels_kernel, tuple(masks)),
        out_shape=jax.ShapeDtypeStruct((count, rows, width), state.dtype),
        grid_spec=pltpu.PrefetchScalarGridSpec(
            num_scalar_prefetch=1,
            grid=(n_levels,),
            in_specs=[
                pl.BlockSpec((1,) + trp.shape[1:], lambda i, p: (level_offset + i, 0, 0, 0, 0, 0)),
                pl.BlockSpec(block, lambda i, p: index_of),
            ],
            out_specs=pl.BlockSpec((count, rows, width), lambda i, p: (0, 0, 0)),
            scratch_shapes=[
                pltpu.VMEM((patterns, 2, 2 * rank, 2 * rank), jnp.float32),
                pltpu.VMEM((2, count, rows, width), jnp.float32),
            ],
        ),
        compiler_params=pltpu.CompilerParams(vmem_limit_bytes=48 * 1024 * 1024),
        cost_estimate=pl.CostEstimate(
            flops=flops, transcendentals=0, bytes_accessed=2 * count * rows * width * 4 + n_levels * trp[0].size * 4
        ),
    )(pidx, trp, state)


def place_kernel(x_ref, *refs):
    refs[-1][...] = x_ref[...]


def place_piece(piece, out, parity, chunk, split, k_len):
    count, rows, width = piece.shape
    step = 4 if count % 4 == 0 else 1
    in_specs = [pl.BlockSpec((step, rows, width), lambda i: (i, 0, 0))]
    args = [piece]
    aliases = {}
    if out is not None:
        in_specs.append(pl.BlockSpec(memory_space=pl.ANY))
        args.append(out)
        aliases = {1: 0}
    return pl.pallas_call(
        place_kernel,
        out_shape=jax.ShapeDtypeStruct((count, split, rows, k_len), piece.dtype),
        grid=(count // step,),
        in_specs=in_specs,
        out_specs=pl.BlockSpec((step, None, rows, width), lambda i: (i, parity, 0, chunk)),
        input_output_aliases=aliases,
        cost_estimate=pl.CostEstimate(flops=0, transcendentals=0, bytes_accessed=2 * piece.size * 4),
    )(*args)


def body(weights_in, translations, pattern_index):
    box_count, rows, k_len = weights_in.shape
    groups = lax.axis_size("src")
    local_bits = box_count.bit_length() - 1
    top_bits = (box_count * groups).bit_length() - 1
    device = lax.axis_index("src")
    bits = [top_bits - LEVELS + level for level in range(LEVELS)]
    first_cross = next((lv for lv, b in enumerate(bits) if b >= local_bits), LEVELS)

    split = 2 if (PARITY_SPLIT and bits[0] >= 1 and box_count // 2 >= groups) else 1
    split_bits = split.bit_length() - 1
    count = box_count // split
    repeat = count // groups
    repeat_bits = repeat.bit_length() - 1
    k_chunks = 1 if split > 1 else K_CHUNKS
    width = k_len // k_chunks
    shaped = weights_in.reshape(count, split, rows, k_len) if split > 1 else weights_in

    slot = jnp.arange(count, dtype=jnp.int32)
    local_masks = [1 << (bits[lv] - split_bits) for lv in range(first_cross)]
    cross_masks = [1 << (bits[lv] - local_bits + repeat_bits) for lv in range(first_cross, LEVELS)]

    pieces = {}
    for parity in range(split):
        own_boxes = device * box_count + slot * split + parity
        held_boxes = slot // repeat * box_count + (device * repeat + slot % repeat) * split + parity
        local_pidx = jnp.take(pattern_index[:first_cross], own_boxes, axis=1)
        cross_pidx = jnp.take(pattern_index[first_cross:], held_boxes, axis=1)
        for chunk in range(k_chunks):
            index_of = (0, parity, 0, chunk) if split > 1 else (0, 0, chunk)
            if first_cross > 0:
                state = apply_levels(shaped, translations, local_pidx, local_masks, 0, index_of, count, width)
            elif split > 1:
                state = shaped[:, parity, :, chunk * width : (chunk + 1) * width]
            else:
                state = shaped[:, :, chunk * width : (chunk + 1) * width]
            current = lax.all_to_all(state, "src", split_axis=0, concat_axis=0, tiled=True)
            current = apply_levels(
                current, translations, cross_pidx, cross_masks, first_cross, (0, 0, 0), count, width
            )
            pieces[parity, chunk] = lax.all_to_all(current, "src", split_axis=0, concat_axis=0, tiled=True)
    out = None
    for parity, chunk in sorted(pieces):
        out = place_piece(pieces[parity, chunk], out, parity, chunk, split, k_len)
    return out.reshape(box_count, rows, k_len)


def solution(mesh):
    placed = (P(("shots", "src"), None, None), P(), P())
    return jax.shard_map(
        body, mesh=mesh, in_specs=placed, out_specs=P(("shots", "src"), None, None), check_vma=False
    )
```

```python
import functools

import jax
import jax.numpy as jnp
from jax import lax
from jax.experimental import pallas as pl
from jax.experimental.pallas import tpu as pltpu
from jax.sharding import PartitionSpec as P

LEVELS = 8
K_CHUNKS = 2
PARITY_SPLIT = True


def levels_kernel(masks, pidx_ref, tr_ref, x_ref, o_ref, table, buf):
    level = pl.program_id(0)
    patterns = tr_ref.shape[1]
    rank = tr_ref.shape[-1]
    for p in range(patterns):
        for j in range(2):
            re = tr_ref[0, p, j, 0]
            im = tr_ref[0, p, j, 1]
            table[p, j, 0:rank] = jnp.concatenate([re, -im], axis=1)
            table[p, j, rank : 2 * rank] = jnp.concatenate([im, re], axis=1)

    count = x_ref.shape[0]
    last = len(masks) - 1
    for li, mask in enumerate(masks):
        src = x_ref if li == 0 else buf.at[(li - 1) % 2]
        dst = o_ref if li == last else buf.at[li % 2]

        @pl.when(level == li)
        def _(src=src, dst=dst, li=li, mask=mask):
            def pair(i, carry):
                lo = (i // mask) * (2 * mask) + i % mask
                hi = lo + mask
                p_lo = pidx_ref[li, lo]
                p_hi = pidx_ref[li, hi]
                lhs = jnp.concatenate(
                    [
                        jnp.concatenate([table[p_lo, 0], table[p_lo, 1]], axis=1),
                        jnp.concatenate([table[p_hi, 1], table[p_hi, 0]], axis=1),
                    ],
                    axis=0,
                )
                rhs = jnp.concatenate([src[lo], src[hi]], axis=0)
                out = jnp.dot(lhs, rhs, precision=lax.Precision.HIGHEST, preferred_element_type=jnp.float32)
                half = out.shape[0] // 2
                dst[lo] = out[:half]
                dst[hi] = out[half:]
                return carry

            lax.fori_loop(0, count // 2, pair, 0)


def apply_levels(state, trp, pidx, masks, level_offset, index_of, count, width):
    rows = state.shape[-2]
    n_levels = len(masks)
    patterns = trp.shape[1]
    rank = trp.shape[-1]
    block = (count, None, rows, width) if state.ndim == 4 else (count, rows, width)
    flops = 2 * count * rows * 2 * rows * width * n_levels
    return pl.pallas_call(
        functools.partial(levels_kernel, tuple(masks)),
        out_shape=jax.ShapeDtypeStruct((count, rows, width), state.dtype),
        grid_spec=pltpu.PrefetchScalarGridSpec(
            num_scalar_prefetch=1,
            grid=(n_levels,),
            in_specs=[
                pl.BlockSpec((1,) + trp.shape[1:], lambda i, p: (level_offset + i, 0, 0, 0, 0, 0)),
                pl.BlockSpec(block, lambda i, p: index_of)
                if state.shape != (count, rows, width)
                else pl.BlockSpec(memory_space=pltpu.VMEM),
            ],
            out_specs=pl.BlockSpec(memory_space=pltpu.VMEM),
            scratch_shapes=[
                pltpu.VMEM((patterns, 2, 2 * rank, 2 * rank), jnp.float32),
                pltpu.VMEM((2, count, rows, width), jnp.float32),
            ],
        ),
        compiler_params=pltpu.CompilerParams(vmem_limit_bytes=48 * 1024 * 1024),
        cost_estimate=pl.CostEstimate(
            flops=flops, transcendentals=0, bytes_accessed=2 * count * rows * width * 4 + n_levels * trp[0].size * 4
        ),
    )(pidx, trp, state)


def place_kernel(step, x_ref, *refs):
    start = pl.multiple_of(pl.program_id(0) * step, step)
    refs[-1][...] = x_ref[pl.ds(start, step)]


def place_piece(piece, out, parity, chunk, split, k_len):
    count, rows, width = piece.shape
    step = count // 2 if count % 2 == 0 else count
    in_specs = [pl.BlockSpec(memory_space=pltpu.VMEM)]
    args = [piece]
    aliases = {}
    if out is not None:
        in_specs.append(pl.BlockSpec(memory_space=pl.ANY))
        args.append(out)
        aliases = {1: 0}
    return pl.pallas_call(
        functools.partial(place_kernel, step),
        out_shape=jax.ShapeDtypeStruct((count, split, rows, k_len), piece.dtype),
        grid=(count // step,),
        in_specs=in_specs,
        out_specs=pl.BlockSpec((step, None, rows, width), lambda i: (i, parity, 0, chunk)),
        input_output_aliases=aliases,
        cost_estimate=pl.CostEstimate(flops=0, transcendentals=0, bytes_accessed=2 * piece.size * 4),
    )(*args)


def body(weights_in, translations, pattern_index):
    box_count, rows, k_len = weights_in.shape
    groups = lax.axis_size("src")
    local_bits = box_count.bit_length() - 1
    top_bits = (box_count * groups).bit_length() - 1
    device = lax.axis_index("src")
    bits = [top_bits - LEVELS + level for level in range(LEVELS)]
    first_cross = next((lv for lv, b in enumerate(bits) if b >= local_bits), LEVELS)

    split = 2 if (PARITY_SPLIT and bits[0] >= 1 and box_count // 2 >= groups) else 1
    split_bits = split.bit_length() - 1
    count = box_count // split
    repeat = count // groups
    repeat_bits = repeat.bit_length() - 1
    k_chunks = 1 if split > 1 else K_CHUNKS
    width = k_len // k_chunks
    shaped = weights_in.reshape(count, split, rows, k_len) if split > 1 else weights_in

    slot = jnp.arange(count, dtype=jnp.int32)
    local_masks = [1 << (bits[lv] - split_bits) for lv in range(first_cross)]
    cross_masks = [1 << (bits[lv] - local_bits + repeat_bits) for lv in range(first_cross, LEVELS)]

    pieces = {}
    for parity in range(split):
        own_boxes = device * box_count + slot * split + parity
        held_boxes = slot // repeat * box_count + (device * repeat + slot % repeat) * split + parity
        local_pidx = jnp.take(pattern_index[:first_cross], own_boxes, axis=1)
        cross_pidx = jnp.take(pattern_index[first_cross:], held_boxes, axis=1)
        for chunk in range(k_chunks):
            index_of = (0, parity, 0, chunk) if split > 1 else (0, 0, chunk)
            if first_cross > 0:
                state = apply_levels(shaped, translations, local_pidx, local_masks, 0, index_of, count, width)
            elif split > 1:
                state = shaped[:, parity, :, chunk * width : (chunk + 1) * width]
            else:
                state = shaped[:, :, chunk * width : (chunk + 1) * width]
            current = lax.all_to_all(state, "src", split_axis=0, concat_axis=0, tiled=True)
            current = apply_levels(
                current, translations, cross_pidx, cross_masks, first_cross, (0, 0, 0), count, width
            )
            pieces[parity, chunk] = lax.all_to_all(current, "src", split_axis=0, concat_axis=0, tiled=True)
    out = None
    for parity, chunk in sorted(pieces):
        out = place_piece(pieces[parity, chunk], out, parity, chunk, split, k_len)
    return out.reshape(box_count, rows, k_len)


def solution(mesh):
    placed = (P(("shots", "src"), None, None), P(), P())
    return jax.shard_map(
        body, mesh=mesh, in_specs=placed, out_specs=P(("shots", "src"), None, None), check_vma=False
    )
```

```python
import functools

import jax
import jax.numpy as jnp
from jax import lax
from jax.experimental import pallas as pl
from jax.experimental.pallas import tpu as pltpu
from jax.sharding import PartitionSpec as P

LEVELS = 8
K_CHUNKS = 2
PARITY_SPLIT = True


def levels_kernel(masks, pidx_ref, tr_ref, x_ref, o_ref, table, buf):
    level = pl.program_id(0)
    patterns = tr_ref.shape[1]
    rank = tr_ref.shape[-1]
    for p in range(patterns):
        for j in range(2):
            re = tr_ref[0, p, j, 0]
            im = tr_ref[0, p, j, 1]
            table[p, j, 0:rank] = jnp.concatenate([re, -im], axis=1)
            table[p, j, rank : 2 * rank] = jnp.concatenate([im, re], axis=1)

    count = x_ref.shape[0]
    last = len(masks) - 1
    for li, mask in enumerate(masks):
        src = x_ref if li == 0 else buf.at[(li - 1) % 2]
        dst = o_ref if li == last else buf.at[li % 2]

        @pl.when(level == li)
        def _(src=src, dst=dst, li=li, mask=mask):
            def pair(i, carry):
                lo = (i // mask) * (2 * mask) + i % mask
                hi = lo + mask
                p_lo = pidx_ref[li, lo]
                p_hi = pidx_ref[li, hi]
                lhs = jnp.concatenate(
                    [
                        jnp.concatenate([table[p_lo, 0], table[p_lo, 1]], axis=1),
                        jnp.concatenate([table[p_hi, 1], table[p_hi, 0]], axis=1),
                    ],
                    axis=0,
                )
                rhs = jnp.concatenate([src[lo], src[hi]], axis=0)
                out = jnp.dot(lhs, rhs, precision=lax.Precision.HIGHEST, preferred_element_type=jnp.float32)
                half = out.shape[0] // 2
                dst[lo] = out[:half]
                dst[hi] = out[half:]
                return carry

            lax.fori_loop(0, count // 2, pair, 0)


def apply_levels(state, trp, pidx, masks, level_offset, index_of, count, width):
    rows = state.shape[-2]
    n_levels = len(masks)
    patterns = trp.shape[1]
    rank = trp.shape[-1]
    block = (count, None, rows, width) if state.ndim == 4 else (count, rows, width)
    flops = 2 * count * rows * 2 * rows * width * n_levels
    return pl.pallas_call(
        functools.partial(levels_kernel, tuple(masks)),
        out_shape=jax.ShapeDtypeStruct((count, rows, width), state.dtype),
        grid_spec=pltpu.PrefetchScalarGridSpec(
            num_scalar_prefetch=1,
            grid=(n_levels,),
            in_specs=[
                pl.BlockSpec((1,) + trp.shape[1:], lambda i, p: (level_offset + i, 0, 0, 0, 0, 0)),
                pl.BlockSpec(block, lambda i, p: index_of)
                if state.shape != (count, rows, width)
                else pl.BlockSpec(memory_space=pltpu.VMEM),
            ],
            out_specs=pl.BlockSpec(memory_space=pltpu.VMEM),
            scratch_shapes=[
                pltpu.VMEM((patterns, 2, 2 * rank, 2 * rank), jnp.float32),
                pltpu.VMEM((2, count, rows, width), jnp.float32),
            ],
        ),
        compiler_params=pltpu.CompilerParams(vmem_limit_bytes=48 * 1024 * 1024),
        cost_estimate=pl.CostEstimate(
            flops=flops, transcendentals=0, bytes_accessed=2 * count * rows * width * 4 + n_levels * trp[0].size * 4
        ),
    )(pidx, trp, state)


def place_kernel(step, x_ref, *refs):
    start = pl.multiple_of(pl.program_id(0) * step, step)
    refs[-1][...] = x_ref[pl.ds(start, step)]


def place_piece(piece, out, parity, chunk, split, k_len):
    count, rows, width = piece.shape
    step = count // 2 if count % 2 == 0 else count
    in_specs = [pl.BlockSpec(memory_space=pltpu.VMEM)]
    args = [piece]
    aliases = {}
    if out is not None:
        in_specs.append(pl.BlockSpec(memory_space=pl.ANY))
        args.append(out)
        aliases = {1: 0}
    return pl.pallas_call(
        functools.partial(place_kernel, step),
        out_shape=jax.ShapeDtypeStruct((count, split, rows, k_len), piece.dtype),
        grid=(count // step,),
        in_specs=in_specs,
        out_specs=pl.BlockSpec((step, None, rows, width), lambda i: (i, parity, 0, chunk)),
        input_output_aliases=aliases,
        cost_estimate=pl.CostEstimate(flops=0, transcendentals=0, bytes_accessed=2 * piece.size * 4),
    )(*args)


def body(weights_in, translations, pattern_index):
    box_count, rows, k_len = weights_in.shape
    groups = lax.axis_size("src")
    local_bits = box_count.bit_length() - 1
    top_bits = (box_count * groups).bit_length() - 1
    device = lax.axis_index("src")
    bits = [top_bits - LEVELS + level for level in range(LEVELS)]
    first_cross = next((lv for lv, b in enumerate(bits) if b >= local_bits), LEVELS)

    split = 2 if (PARITY_SPLIT and bits[0] >= 1 and box_count // 2 >= groups) else 1
    split_bits = split.bit_length() - 1
    count = box_count // split
    repeat = count // groups
    repeat_bits = repeat.bit_length() - 1
    k_chunks = 1 if split > 1 else K_CHUNKS
    width = k_len // k_chunks
    shaped = weights_in.reshape(count, split, rows, k_len) if split > 1 else weights_in

    slot = jnp.arange(count, dtype=jnp.int32)
    local_masks = [1 << (bits[lv] - split_bits) for lv in range(first_cross)]
    cross_masks = [1 << (bits[lv] - local_bits + repeat_bits) for lv in range(first_cross, LEVELS)]

    pieces = {}
    for parity in range(split):
        own_boxes = device * box_count + slot * split + parity
        held_boxes = slot // repeat * box_count + (device * repeat + slot % repeat) * split + parity
        local_pidx = jnp.take(pattern_index[:first_cross], own_boxes, axis=1)
        cross_pidx = jnp.take(pattern_index[first_cross:], held_boxes, axis=1)
        for chunk in range(k_chunks):
            index_of = (0, parity, 0, chunk) if split > 1 else (0, 0, chunk)
            if first_cross > 0:
                state = apply_levels(shaped, translations, local_pidx, local_masks, 0, index_of, count, width)
            elif split > 1:
                state = shaped[:, parity, :, chunk * width : (chunk + 1) * width]
            else:
                state = shaped[:, :, chunk * width : (chunk + 1) * width]
            current = lax.all_to_all(state, "src", split_axis=0, concat_axis=0, tiled=True)
            current = apply_levels(
                current, translations, cross_pidx, cross_masks, first_cross, (0, 0, 0), count, width
            )
            pieces[parity, chunk] = lax.all_to_all(current, "src", split_axis=0, concat_axis=0, tiled=True)
    order = sorted(pieces)
    out = None
    for parity, chunk in order[:-1]:
        out = place_piece(pieces[parity, chunk], out, parity, chunk, split, k_len)
    parity, chunk = order[-1]
    if out is None:
        out = jnp.zeros((count, split, rows, k_len), weights_in.dtype)
    out = out.at[:, parity, :, chunk * width : (chunk + 1) * width].set(pieces[parity, chunk])
    return out.reshape(box_count, rows, k_len)


def solution(mesh):
    placed = (P(("shots", "src"), None, None), P(), P())
    return jax.shard_map(
        body, mesh=mesh, in_specs=placed, out_specs=P(("shots", "src"), None, None), check_vma=False
    )
```

```python
import functools

import jax
import jax.numpy as jnp
from jax import lax
from jax.experimental import pallas as pl
from jax.experimental.pallas import tpu as pltpu
from jax.sharding import PartitionSpec as P

LEVELS = 8
K_CHUNKS = 2
PARITY_SPLIT = True


def levels_kernel(masks, level_offset, layout, pidx_ref, tr_ref, x_ref, o_ref, table, buf):
    level = pl.program_id(0)
    patterns = tr_ref.shape[1]
    rank = tr_ref.shape[-1]
    for p in range(patterns):
        for j in range(2):
            re = tr_ref[0, p, j, 0]
            im = tr_ref[0, p, j, 1]
            table[p, j, 0:rank] = jnp.concatenate([re, -im], axis=1)
            table[p, j, rank : 2 * rank] = jnp.concatenate([im, re], axis=1)

    count = x_ref.shape[0]
    last = len(masks) - 1
    box_count, split, parity, repeat = layout
    device = lax.axis_index("src")

    def box_of(slot):
        return (slot // repeat) * box_count + (device * repeat + slot % repeat) * split + parity

    for li, mask in enumerate(masks):
        src = x_ref if li == 0 else buf.at[(li - 1) % 2]
        dst = o_ref if li == last else buf.at[li % 2]

        @pl.when(level == li)
        def _(src=src, dst=dst, li=li, mask=mask):
            def pair(i, carry):
                lo = (i // mask) * (2 * mask) + i % mask
                hi = lo + mask
                p_lo = pidx_ref[level_offset + li, box_of(lo)]
                p_hi = pidx_ref[level_offset + li, box_of(hi)]
                lhs = jnp.concatenate(
                    [
                        jnp.concatenate([table[p_lo, 0], table[p_lo, 1]], axis=1),
                        jnp.concatenate([table[p_hi, 1], table[p_hi, 0]], axis=1),
                    ],
                    axis=0,
                )
                rhs = jnp.concatenate([src[lo], src[hi]], axis=0)
                out = jnp.dot(lhs, rhs, precision=lax.Precision.HIGHEST, preferred_element_type=jnp.float32)
                half = out.shape[0] // 2
                dst[lo] = out[:half]
                dst[hi] = out[half:]
                return carry

            lax.fori_loop(0, count // 2, pair, 0)


def apply_levels(state, trp, pidx, masks, level_offset, layout, index_of, count, width):
    rows = state.shape[-2]
    n_levels = len(masks)
    patterns = trp.shape[1]
    rank = trp.shape[-1]
    block = (count, None, rows, width) if state.ndim == 4 else (count, rows, width)
    flops = 2 * count * rows * 2 * rows * width * n_levels
    return pl.pallas_call(
        functools.partial(levels_kernel, tuple(masks), level_offset, layout),
        out_shape=jax.ShapeDtypeStruct((count, rows, width), state.dtype),
        grid_spec=pltpu.PrefetchScalarGridSpec(
            num_scalar_prefetch=1,
            grid=(n_levels,),
            in_specs=[
                pl.BlockSpec((1,) + trp.shape[1:], lambda i, p: (level_offset + i, 0, 0, 0, 0, 0)),
                pl.BlockSpec(block, lambda i, p: index_of)
                if state.shape != (count, rows, width)
                else pl.BlockSpec(memory_space=pltpu.VMEM),
            ],
            out_specs=pl.BlockSpec(memory_space=pltpu.VMEM),
            scratch_shapes=[
                pltpu.VMEM((patterns, 2, 2 * rank, 2 * rank), jnp.float32),
                pltpu.VMEM((2, count, rows, width), jnp.float32),
            ],
        ),
        compiler_params=pltpu.CompilerParams(vmem_limit_bytes=48 * 1024 * 1024),
        cost_estimate=pl.CostEstimate(
            flops=flops, transcendentals=0, bytes_accessed=2 * count * rows * width * 4 + n_levels * trp[0].size * 4
        ),
    )(pidx, trp, state)


def place_kernel(step, x_ref, *refs):
    start = pl.multiple_of(pl.program_id(0) * step, step)
    refs[-1][...] = x_ref[pl.ds(start, step)]


def place_piece(piece, out, parity, chunk, split, k_len):
    count, rows, width = piece.shape
    step = count // 2 if count % 2 == 0 else count
    in_specs = [pl.BlockSpec(memory_space=pltpu.VMEM)]
    args = [piece]
    aliases = {}
    if out is not None:
        in_specs.append(pl.BlockSpec(memory_space=pl.ANY))
        args.append(out)
        aliases = {1: 0}
    return pl.pallas_call(
        functools.partial(place_kernel, step),
        out_shape=jax.ShapeDtypeStruct((count, split, rows, k_len), piece.dtype),
        grid=(count // step,),
        in_specs=in_specs,
        out_specs=pl.BlockSpec((step, None, rows, width), lambda i: (i, parity, 0, chunk)),
        input_output_aliases=aliases,
        cost_estimate=pl.CostEstimate(flops=0, transcendentals=0, bytes_accessed=2 * piece.size * 4),
    )(*args)


def body(weights_in, translations, pattern_index):
    box_count, rows, k_len = weights_in.shape
    groups = lax.axis_size("src")
    local_bits = box_count.bit_length() - 1
    top_bits = (box_count * groups).bit_length() - 1
    device = lax.axis_index("src")
    bits = [top_bits - LEVELS + level for level in range(LEVELS)]
    first_cross = next((lv for lv, b in enumerate(bits) if b >= local_bits), LEVELS)

    split = 2 if (PARITY_SPLIT and bits[0] >= 1 and box_count // 2 >= groups) else 1
    split_bits = split.bit_length() - 1
    count = box_count // split
    repeat = count // groups
    repeat_bits = repeat.bit_length() - 1
    k_chunks = 1 if split > 1 else K_CHUNKS
    width = k_len // k_chunks
    shaped = weights_in.reshape(count, split, rows, k_len) if split > 1 else weights_in

    local_masks = [1 << (bits[lv] - split_bits) for lv in range(first_cross)]
    cross_masks = [1 << (bits[lv] - local_bits + repeat_bits) for lv in range(first_cross, LEVELS)]

    pieces = {}
    for parity in range(split):
        local_layout = (box_count, split, parity, count)
        cross_layout = (box_count, split, parity, repeat)
        for chunk in range(k_chunks):
            index_of = (0, parity, 0, chunk) if split > 1 else (0, 0, chunk)
            if first_cross > 0:
                state = apply_levels(shaped, translations, pattern_index, local_masks, 0, local_layout, index_of, count, width)
            elif split > 1:
                state = shaped[:, parity, :, chunk * width : (chunk + 1) * width]
            else:
                state = shaped[:, :, chunk * width : (chunk + 1) * width]
            current = lax.all_to_all(state, "src", split_axis=0, concat_axis=0, tiled=True)
            current = apply_levels(
                current, translations, pattern_index, cross_masks, first_cross, cross_layout, (0, 0, 0), count, width
            )
            pieces[parity, chunk] = lax.all_to_all(current, "src", split_axis=0, concat_axis=0, tiled=True)
    order = sorted(pieces)
    out = None
    for parity, chunk in order[:-1]:
        out = place_piece(pieces[parity, chunk], out, parity, chunk, split, k_len)
    parity, chunk = order[-1]
    if out is None:
        out = jnp.zeros((count, split, rows, k_len), weights_in.dtype)
    out = out.at[:, parity, :, chunk * width : (chunk + 1) * width].set(pieces[parity, chunk])
    return out.reshape(box_count, rows, k_len)


def solution(mesh):
    placed = (P(("shots", "src"), None, None), P(), P())
    return jax.shard_map(
        body, mesh=mesh, in_specs=placed, out_specs=P(("shots", "src"), None, None), check_vma=False
    )
```

```python
import functools

import jax
import jax.numpy as jnp
from jax import lax
from jax.experimental import pallas as pl
from jax.experimental.pallas import tpu as pltpu
from jax.sharding import PartitionSpec as P

LEVELS = 8
K_CHUNKS = 2
PARITY_SPLIT = True


def levels_kernel(masks, level_offset, layout, precision, pidx_ref, tr_ref, x_ref, o_ref, table, buf):
    level = pl.program_id(0)
    patterns = tr_ref.shape[1]
    rank = tr_ref.shape[-1]
    for p in range(patterns):
        for j in range(2):
            re = tr_ref[0, p, j, 0]
            im = tr_ref[0, p, j, 1]
            table[p, j, 0:rank] = jnp.concatenate([re, -im], axis=1)
            table[p, j, rank : 2 * rank] = jnp.concatenate([im, re], axis=1)

    count = x_ref.shape[0]
    last = len(masks) - 1
    box_count, split, parity, repeat = layout
    device = lax.axis_index("src")

    def box_of(slot):
        return (slot // repeat) * box_count + (device * repeat + slot % repeat) * split + parity

    for li, mask in enumerate(masks):
        src = x_ref if li == 0 else buf.at[(li - 1) % 2]
        dst = o_ref if li == last else buf.at[li % 2]

        @pl.when(level == li)
        def _(src=src, dst=dst, li=li, mask=mask):
            def pair(i, carry):
                lo = (i // mask) * (2 * mask) + i % mask
                hi = lo + mask
                p_lo = pidx_ref[level_offset + li, box_of(lo)]
                p_hi = pidx_ref[level_offset + li, box_of(hi)]
                lhs = jnp.concatenate(
                    [
                        jnp.concatenate([table[p_lo, 0], table[p_lo, 1]], axis=1),
                        jnp.concatenate([table[p_hi, 1], table[p_hi, 0]], axis=1),
                    ],
                    axis=0,
                )
                rhs = jnp.concatenate([src[lo], src[hi]], axis=0)
                out = jnp.dot(lhs, rhs, precision=precision, preferred_element_type=jnp.float32)
                half = out.shape[0] // 2
                dst[lo] = out[:half]
                dst[hi] = out[half:]
                return carry

            lax.fori_loop(0, count // 2, pair, 0)


def apply_levels(state, trp, pidx, masks, level_offset, layout, index_of, count, width, precision):
    rows = state.shape[-2]
    n_levels = len(masks)
    patterns = trp.shape[1]
    rank = trp.shape[-1]
    block = (count, None, rows, width) if state.ndim == 4 else (count, rows, width)
    flops = 2 * count * rows * 2 * rows * width * n_levels
    return pl.pallas_call(
        functools.partial(levels_kernel, tuple(masks), level_offset, layout, precision),
        out_shape=jax.ShapeDtypeStruct((count, rows, width), state.dtype),
        grid_spec=pltpu.PrefetchScalarGridSpec(
            num_scalar_prefetch=1,
            grid=(n_levels,),
            in_specs=[
                pl.BlockSpec((1,) + trp.shape[1:], lambda i, p: (level_offset + i, 0, 0, 0, 0, 0)),
                pl.BlockSpec(block, lambda i, p: index_of)
                if state.shape != (count, rows, width)
                else pl.BlockSpec(memory_space=pltpu.VMEM),
            ],
            out_specs=pl.BlockSpec(memory_space=pltpu.VMEM),
            scratch_shapes=[
                pltpu.VMEM((patterns, 2, 2 * rank, 2 * rank), jnp.float32),
                pltpu.VMEM((2, count, rows, width), jnp.float32),
            ],
        ),
        compiler_params=pltpu.CompilerParams(vmem_limit_bytes=48 * 1024 * 1024),
        cost_estimate=pl.CostEstimate(
            flops=flops, transcendentals=0, bytes_accessed=2 * count * rows * width * 4 + n_levels * trp[0].size * 4
        ),
    )(pidx, trp, state)


def place_kernel(step, x_ref, *refs):
    start = pl.multiple_of(pl.program_id(0) * step, step)
    refs[-1][...] = x_ref[pl.ds(start, step)]


def place_piece(piece, out, parity, chunk, split, k_len):
    count, rows, width = piece.shape
    step = count // 2 if count % 2 == 0 else count
    in_specs = [pl.BlockSpec(memory_space=pltpu.VMEM)]
    args = [piece]
    aliases = {}
    if out is not None:
        in_specs.append(pl.BlockSpec(memory_space=pl.ANY))
        args.append(out)
        aliases = {1: 0}
    return pl.pallas_call(
        functools.partial(place_kernel, step),
        out_shape=jax.ShapeDtypeStruct((count, split, rows, k_len), piece.dtype),
        grid=(count // step,),
        in_specs=in_specs,
        out_specs=pl.BlockSpec((step, None, rows, width), lambda i: (i, parity, 0, chunk)),
        input_output_aliases=aliases,
        cost_estimate=pl.CostEstimate(flops=0, transcendentals=0, bytes_accessed=2 * piece.size * 4),
    )(*args)


def body(weights_in, translations, pattern_index):
    box_count, rows, k_len = weights_in.shape
    groups = lax.axis_size("src")
    local_bits = box_count.bit_length() - 1
    top_bits = (box_count * groups).bit_length() - 1
    device = lax.axis_index("src")
    bits = [top_bits - LEVELS + level for level in range(LEVELS)]
    first_cross = next((lv for lv, b in enumerate(bits) if b >= local_bits), LEVELS)

    split = 2 if (PARITY_SPLIT and bits[0] >= 1 and box_count // 2 >= groups) else 1
    split_bits = split.bit_length() - 1
    count = box_count // split
    repeat = count // groups
    repeat_bits = repeat.bit_length() - 1
    k_chunks = 1 if split > 1 else K_CHUNKS
    width = k_len // k_chunks
    shaped = weights_in.reshape(count, split, rows, k_len) if split > 1 else weights_in

    local_masks = [1 << (bits[lv] - split_bits) for lv in range(first_cross)]
    cross_masks = [1 << (bits[lv] - local_bits + repeat_bits) for lv in range(first_cross, LEVELS)]

    pieces = {}
    for parity in range(split):
        local_layout = (box_count, split, parity, count)
        cross_layout = (box_count, split, parity, repeat)
        for chunk in range(k_chunks):
            index_of = (0, parity, 0, chunk) if split > 1 else (0, 0, chunk)
            if first_cross > 0:
                state = apply_levels(
                    shaped, translations, pattern_index, local_masks, 0, local_layout, index_of, count, width,
                    lax.Precision.HIGH if (parity, chunk) == (0, 0) else lax.Precision.HIGHEST,
                )
            elif split > 1:
                state = shaped[:, parity, :, chunk * width : (chunk + 1) * width]
            else:
                state = shaped[:, :, chunk * width : (chunk + 1) * width]
            current = lax.all_to_all(state, "src", split_axis=0, concat_axis=0, tiled=True)
            current = apply_levels(
                current, translations, pattern_index, cross_masks, first_cross, cross_layout, (0, 0, 0), count, width,
                lax.Precision.HIGHEST,
            )
            pieces[parity, chunk] = lax.all_to_all(current, "src", split_axis=0, concat_axis=0, tiled=True)
    order = sorted(pieces)
    out = None
    for parity, chunk in order[:-1]:
        out = place_piece(pieces[parity, chunk], out, parity, chunk, split, k_len)
    parity, chunk = order[-1]
    if out is None:
        out = jnp.zeros((count, split, rows, k_len), weights_in.dtype)
    out = out.at[:, parity, :, chunk * width : (chunk + 1) * width].set(pieces[parity, chunk])
    return out.reshape(box_count, rows, k_len)


def solution(mesh):
    placed = (P(("shots", "src"), None, None), P(), P())
    return jax.shard_map(
        body, mesh=mesh, in_specs=placed, out_specs=P(("shots", "src"), None, None), check_vma=False
    )
```

```python
import functools

import jax
import jax.numpy as jnp
from jax import lax
from jax.experimental import pallas as pl
from jax.experimental.pallas import tpu as pltpu
from jax.sharding import PartitionSpec as P

LEVELS = 8
K_CHUNKS = 2
PARITY_SPLIT = True


def levels_kernel(masks, level_offset, layout, precision, unroll, pidx_ref, tr_ref, x_ref, o_ref, table, buf_a, buf_b):
    level = pl.program_id(0)
    patterns = tr_ref.shape[1]
    rank = tr_ref.shape[-1]
    for p in range(patterns):
        for j in range(2):
            re = tr_ref[0, p, j, 0]
            im = tr_ref[0, p, j, 1]
            table[p, j, 0:rank] = jnp.concatenate([re, -im], axis=1)
            table[p, j, rank : 2 * rank] = jnp.concatenate([im, re], axis=1)

    count = x_ref.shape[0]
    last = len(masks) - 1
    box_count, split, parity, repeat = layout
    device = lax.axis_index("src")

    def box_of(slot):
        return (slot // repeat) * box_count + (device * repeat + slot % repeat) * split + parity

    for li, mask in enumerate(masks):
        src = x_ref if li == 0 else (buf_a if (li - 1) % 2 == 0 else buf_b)
        dst = o_ref if li == last else (buf_a if li % 2 == 0 else buf_b)

        @pl.when(level == li)
        def _(src=src, dst=dst, li=li, mask=mask):
            def pair(i, carry):
                lo = (i // mask) * (2 * mask) + i % mask
                hi = lo + mask
                p_lo = pidx_ref[level_offset + li, box_of(lo)]
                p_hi = pidx_ref[level_offset + li, box_of(hi)]
                lhs = jnp.concatenate(
                    [
                        jnp.concatenate([table[p_lo, 0], table[p_lo, 1]], axis=1),
                        jnp.concatenate([table[p_hi, 1], table[p_hi, 0]], axis=1),
                    ],
                    axis=0,
                )
                rhs = jnp.concatenate([src[lo], src[hi]], axis=0)
                out = jnp.dot(lhs, rhs, precision=precision, preferred_element_type=jnp.float32)
                half = out.shape[0] // 2
                dst[lo] = out[:half]
                dst[hi] = out[half:]
                return carry

            lax.fori_loop(0, count // 2, pair, 0, unroll=min(count // 2, unroll))


def apply_levels(state, trp, pidx, masks, level_offset, layout, index_of, count, width, precision, unroll=1):
    rows = state.shape[-2]
    n_levels = len(masks)
    patterns = trp.shape[1]
    rank = trp.shape[-1]
    block = (count, None, rows, width) if state.ndim == 4 else (count, rows, width)
    flops = 2 * count * rows * 2 * rows * width * n_levels
    return pl.pallas_call(
        functools.partial(levels_kernel, tuple(masks), level_offset, layout, precision, unroll),
        out_shape=jax.ShapeDtypeStruct((count, rows, width), state.dtype),
        grid_spec=pltpu.PrefetchScalarGridSpec(
            num_scalar_prefetch=1,
            grid=(n_levels,),
            in_specs=[
                pl.BlockSpec((1,) + trp.shape[1:], lambda i, p: (level_offset + i, 0, 0, 0, 0, 0)),
                pl.BlockSpec(block, lambda i, p: index_of)
                if state.shape != (count, rows, width)
                else pl.BlockSpec(memory_space=pltpu.VMEM),
            ],
            out_specs=pl.BlockSpec(memory_space=pltpu.VMEM),
            scratch_shapes=[
                pltpu.VMEM((patterns, 2, 2 * rank, 2 * rank), jnp.float32),
                pltpu.VMEM((count, rows, width), jnp.float32),
                pltpu.VMEM((count, rows, width), jnp.float32),
            ],
        ),
        compiler_params=pltpu.CompilerParams(vmem_limit_bytes=48 * 1024 * 1024),
        cost_estimate=pl.CostEstimate(
            flops=flops, transcendentals=0, bytes_accessed=2 * count * rows * width * 4 + n_levels * trp[0].size * 4
        ),
    )(pidx, trp, state)


def place_kernel(step, x_ref, *refs):
    start = pl.multiple_of(pl.program_id(0) * step, step)
    refs[-1][...] = x_ref[pl.ds(start, step)]


def place_piece(piece, out, parity, chunk, split, k_len):
    count, rows, width = piece.shape
    step = count // 2 if count % 2 == 0 else count
    in_specs = [pl.BlockSpec(memory_space=pltpu.VMEM)]
    args = [piece]
    aliases = {}
    if out is not None:
        in_specs.append(pl.BlockSpec(memory_space=pl.ANY))
        args.append(out)
        aliases = {1: 0}
    return pl.pallas_call(
        functools.partial(place_kernel, step),
        out_shape=jax.ShapeDtypeStruct((count, split, rows, k_len), piece.dtype),
        grid=(count // step,),
        in_specs=in_specs,
        out_specs=pl.BlockSpec((step, None, rows, width), lambda i: (i, parity, 0, chunk)),
        input_output_aliases=aliases,
        cost_estimate=pl.CostEstimate(flops=0, transcendentals=0, bytes_accessed=2 * piece.size * 4),
    )(*args)


def body(weights_in, translations, pattern_index):
    box_count, rows, k_len = weights_in.shape
    groups = lax.axis_size("src")
    local_bits = box_count.bit_length() - 1
    top_bits = (box_count * groups).bit_length() - 1
    device = lax.axis_index("src")
    bits = [top_bits - LEVELS + level for level in range(LEVELS)]
    first_cross = next((lv for lv, b in enumerate(bits) if b >= local_bits), LEVELS)

    split = 2 if (PARITY_SPLIT and bits[0] >= 1 and box_count // 2 >= groups) else 1
    split_bits = split.bit_length() - 1
    count = box_count // split
    repeat = count // groups
    repeat_bits = repeat.bit_length() - 1
    k_chunks = 1 if split > 1 else K_CHUNKS
    width = k_len // k_chunks
    shaped = weights_in.reshape(count, split, rows, k_len) if split > 1 else weights_in

    local_masks = [1 << (bits[lv] - split_bits) for lv in range(first_cross)]
    cross_masks = [1 << (bits[lv] - local_bits + repeat_bits) for lv in range(first_cross, LEVELS)]

    pieces = {}
    for parity in range(split):
        local_layout = (box_count, split, parity, count)
        cross_layout = (box_count, split, parity, repeat)
        for chunk in range(k_chunks):
            index_of = (0, parity, 0, chunk) if split > 1 else (0, 0, chunk)
            if first_cross > 0:
                state = apply_levels(
                    shaped, translations, pattern_index, local_masks, 0, local_layout, index_of, count, width,
                    lax.Precision.HIGHEST,
                    8 if (parity, chunk) == (0, 0) else 1,
                )
            elif split > 1:
                state = shaped[:, parity, :, chunk * width : (chunk + 1) * width]
            else:
                state = shaped[:, :, chunk * width : (chunk + 1) * width]
            current = lax.all_to_all(state, "src", split_axis=0, concat_axis=0, tiled=True)
            current = apply_levels(
                current, translations, pattern_index, cross_masks, first_cross, cross_layout, (0, 0, 0), count, width,
                lax.Precision.HIGHEST,
            )
            pieces[parity, chunk] = lax.all_to_all(current, "src", split_axis=0, concat_axis=0, tiled=True)
    order = sorted(pieces)
    out = None
    for parity, chunk in order[:-1]:
        out = place_piece(pieces[parity, chunk], out, parity, chunk, split, k_len)
    parity, chunk = order[-1]
    if out is None:
        out = jnp.zeros((count, split, rows, k_len), weights_in.dtype)
    out = out.at[:, parity, :, chunk * width : (chunk + 1) * width].set(pieces[parity, chunk])
    return out.reshape(box_count, rows, k_len)


def solution(mesh):
    placed = (P(("shots", "src"), None, None), P(), P())
    return jax.shard_map(
        body, mesh=mesh, in_specs=placed, out_specs=P(("shots", "src"), None, None), check_vma=False
    )
```

```python
import functools

import jax
import jax.numpy as jnp
from jax import lax
from jax.experimental import pallas as pl
from jax.experimental.pallas import tpu as pltpu
from jax.sharding import PartitionSpec as P

LEVELS = 8
K_CHUNKS = 2
PARITY_SPLIT = True


def levels_kernel(masks, level_offset, layout, precision, unroll, pidx_ref, tr_ref, x_ref, o_ref, table, buf_a, buf_b):
    level = pl.program_id(0)
    patterns = tr_ref.shape[1]
    rank = tr_ref.shape[-1]
    for p in range(patterns):
        for j in range(2):
            re = tr_ref[0, p, j, 0]
            im = tr_ref[0, p, j, 1]
            table[p, j, 0:rank] = jnp.concatenate([re, -im], axis=1)
            table[p, j, rank : 2 * rank] = jnp.concatenate([im, re], axis=1)

    count = x_ref.shape[0]
    last = len(masks) - 1
    box_count, split, parity, repeat = layout
    device = lax.axis_index("src")

    def box_of(slot):
        return (slot // repeat) * box_count + (device * repeat + slot % repeat) * split + parity

    for li, mask in enumerate(masks):
        src = x_ref if li == 0 else (buf_a if (li - 1) % 2 == 0 else buf_b)
        dst = o_ref if li == last else (buf_a if li % 2 == 0 else buf_b)

        @pl.when(level == li)
        def _(src=src, dst=dst, li=li, mask=mask):
            def pair(i, carry):
                lo = (i // mask) * (2 * mask) + i % mask
                hi = lo + mask
                p_lo = pidx_ref[level_offset + li, box_of(lo)]
                p_hi = pidx_ref[level_offset + li, box_of(hi)]
                lhs = jnp.concatenate(
                    [
                        jnp.concatenate([table[p_lo, 0], table[p_lo, 1]], axis=1),
                        jnp.concatenate([table[p_hi, 1], table[p_hi, 0]], axis=1),
                    ],
                    axis=0,
                )
                rhs = jnp.concatenate([src[lo], src[hi]], axis=0)
                out = jnp.dot(lhs, rhs, precision=precision, preferred_element_type=jnp.float32)
                half = out.shape[0] // 2
                dst[lo] = out[:half]
                dst[hi] = out[half:]
                return carry

            lax.fori_loop(0, count // 2, pair, 0, unroll=min(count // 2, unroll))


def apply_levels(state, trp, pidx, masks, level_offset, layout, index_of, count, width, precision, unroll=1):
    rows = state.shape[-2]
    n_levels = len(masks)
    patterns = trp.shape[1]
    rank = trp.shape[-1]
    block = (count, None, rows, width) if state.ndim == 4 else (count, rows, width)
    flops = 2 * count * rows * 2 * rows * width * n_levels
    return pl.pallas_call(
        functools.partial(levels_kernel, tuple(masks), level_offset, layout, precision, unroll),
        out_shape=jax.ShapeDtypeStruct((count, rows, width), state.dtype),
        grid_spec=pltpu.PrefetchScalarGridSpec(
            num_scalar_prefetch=1,
            grid=(n_levels,),
            in_specs=[
                pl.BlockSpec((1,) + trp.shape[1:], lambda i, p: (level_offset + i, 0, 0, 0, 0, 0)),
                pl.BlockSpec(block, lambda i, p: index_of)
                if state.shape != (count, rows, width)
                else pl.BlockSpec(memory_space=pltpu.VMEM),
            ],
            out_specs=pl.BlockSpec(memory_space=pltpu.VMEM),
            scratch_shapes=[
                pltpu.VMEM((patterns, 2, 2 * rank, 2 * rank), jnp.float32),
                pltpu.VMEM((count, rows, width), jnp.float32),
                pltpu.VMEM((count, rows, width), jnp.float32),
            ],
        ),
        compiler_params=pltpu.CompilerParams(vmem_limit_bytes=48 * 1024 * 1024),
        cost_estimate=pl.CostEstimate(
            flops=flops, transcendentals=0, bytes_accessed=2 * count * rows * width * 4 + n_levels * trp[0].size * 4
        ),
    )(pidx, trp, state)


def place_kernel(step, x_ref, *refs):
    start = pl.multiple_of(pl.program_id(0) * step, step)
    refs[-1][...] = x_ref[pl.ds(start, step)]


def place_piece(piece, out, parity, chunk, split, k_len):
    count, rows, width = piece.shape
    step = count // 2 if count % 2 == 0 else count
    in_specs = [pl.BlockSpec(memory_space=pltpu.VMEM)]
    args = [piece]
    aliases = {}
    if out is not None:
        in_specs.append(pl.BlockSpec(memory_space=pl.ANY))
        args.append(out)
        aliases = {1: 0}
    return pl.pallas_call(
        functools.partial(place_kernel, step),
        out_shape=jax.ShapeDtypeStruct((count, split, rows, k_len), piece.dtype),
        grid=(count // step,),
        in_specs=in_specs,
        out_specs=pl.BlockSpec((step, None, rows, width), lambda i: (i, parity, 0, chunk)),
        input_output_aliases=aliases,
        cost_estimate=pl.CostEstimate(flops=0, transcendentals=0, bytes_accessed=2 * piece.size * 4),
    )(*args)


def body(weights_in, translations, pattern_index):
    box_count, rows, k_len = weights_in.shape
    groups = lax.axis_size("src")
    local_bits = box_count.bit_length() - 1
    top_bits = (box_count * groups).bit_length() - 1
    device = lax.axis_index("src")
    bits = [top_bits - LEVELS + level for level in range(LEVELS)]
    first_cross = next((lv for lv, b in enumerate(bits) if b >= local_bits), LEVELS)

    split = 2 if (PARITY_SPLIT and bits[0] >= 1 and box_count // 2 >= groups) else 1
    split_bits = split.bit_length() - 1
    count = box_count // split
    repeat = count // groups
    repeat_bits = repeat.bit_length() - 1
    k_chunks = 1 if split > 1 else K_CHUNKS
    width = k_len // k_chunks
    shaped = weights_in.reshape(count, split, rows, k_len) if split > 1 else weights_in

    local_masks = [1 << (bits[lv] - split_bits) for lv in range(first_cross)]
    cross_masks = [1 << (bits[lv] - local_bits + repeat_bits) for lv in range(first_cross, LEVELS)]

    pieces = {}
    for parity in range(split):
        local_layout = (box_count, split, parity, count)
        cross_layout = (box_count, split, parity, repeat)
        for chunk in range(k_chunks):
            index_of = (0, parity, 0, chunk) if split > 1 else (0, 0, chunk)
            if first_cross > 0:
                state = apply_levels(
                    shaped, translations, pattern_index, local_masks, 0, local_layout, index_of, count, width,
                    lax.Precision.HIGH if (parity, chunk) == (0, 0) else lax.Precision.HIGHEST,
                    8 if (parity, chunk) == (0, 0) else 1,
                )
            elif split > 1:
                state = shaped[:, parity, :, chunk * width : (chunk + 1) * width]
            else:
                state = shaped[:, :, chunk * width : (chunk + 1) * width]
            current = lax.all_to_all(state, "src", split_axis=0, concat_axis=0, tiled=True)
            current = apply_levels(
                current, translations, pattern_index, cross_masks, first_cross, cross_layout, (0, 0, 0), count, width,
                lax.Precision.HIGHEST,
            )
            pieces[parity, chunk] = lax.all_to_all(current, "src", split_axis=0, concat_axis=0, tiled=True)
    order = sorted(pieces)
    out = None
    for parity, chunk in order[:-1]:
        out = place_piece(pieces[parity, chunk], out, parity, chunk, split, k_len)
    parity, chunk = order[-1]
    if out is None:
        out = jnp.zeros((count, split, rows, k_len), weights_in.dtype)
    out = out.at[:, parity, :, chunk * width : (chunk + 1) * width].set(pieces[parity, chunk])
    return out.reshape(box_count, rows, k_len)


def solution(mesh):
    placed = (P(("shots", "src"), None, None), P(), P())
    return jax.shard_map(
        body, mesh=mesh, in_specs=placed, out_specs=P(("shots", "src"), None, None), check_vma=False
    )
```
